256 devices in a mesh: tm: 16 (over x_hi, z), space: 16 (over x_lo, y, core).
Axes of the slice: x: 4 (x_hi: 2, x_lo: 2; x = x_hi * 2 + x_lo), y: 4, z: 8, core: 2. Of those that a mesh axis runs over, the one named last changes fastest.
Arguments:
- start_states: float32 [16, 3, 128, 2048], P('tm', None, 'space'), may hold values from -1.8 to 1.8
- bathymetry: float32 [128, 2048], P('space'), may hold values from 0.5 to 2
- forcing_amp: float32 [128, 2048], P('space'), may hold values from -3 to 3
- land_mask: int32 [128, 2048], P('space'), may hold values 0 or 1
Outputs:
- states: float32 [16, 3, 128, 2048], P('tm', None, 'space')
- grad_states: float32 [16, 3, 128, 2048], P('tm', None, 'space')
- grad_amp: float32 [128, 2048], P('space', 'tm')
- defect_norms: float32 [3], replicated
The draws below stay inside these ranges and needn't reach their ends.
All inputs are finite; a program needn't handle non-finite values. No bound on the sum of `land_mask` on one device may be relied on, other than what follows from the above.
Results may differ from the reference program's by a relative error of at most 0.0003.
Values sent between devices are 32-bit elements; how exact they have to be, the bound alone decides.
No kernel may reach another device: no remote copies, remote signals or barrier semaphores. Data moves between devices by JAX's collectives and lax.ppermute only.
A program may use at most 64 MiB of HBM per device.

```python
import math
import jax
import jax.numpy as jnp
from jax import lax

NY = 2048
STEPS = 2
KRY = 3
NEWTON = 2
SEGS = 16
NX = 128


def draw_start_states(key, part):
    seg_rise = 1.0 + 2.0 * jnp.arange(SEGS).astype(jnp.float32) / (SEGS - 1)
    row_rise = 1.0 + 2.0 * jnp.arange(NX).astype(jnp.float32) / (NX - 1)
    scale = 0.05 * seg_rise[:, None, None, None] * row_rise[None, None, :, None]
    values = jnp.clip(jax.random.normal(key, (SEGS, 3, NX, NY), jnp.float32), -4.0, 4.0)
    return (values * scale).astype(jnp.float32)


def place_ends(values, key, smallest, high):
    longest = values.shape.index(max(values.shape))
    spots = []
    for shift in (0, 1):
        where = [jax.random.randint(jax.random.fold_in(key, axis), (), 0, length) for axis, length in enumerate(values.shape)]
        where[longest] = (where[longest] + shift) % values.shape[longest]
        spots.append(tuple(where))
    return values.at[spots[0]].set(smallest).at[spots[1]].set(high)


def level_of(key, dims, cuts, smallest, high):
    def one(axis_at, blocks):
        draws = jax.random.uniform(jax.random.fold_in(jax.random.fold_in(key, 6), axis_at), (blocks,), jnp.float32, smallest / len(cuts), high / len(cuts))
        return jnp.repeat(jnp.exp(draws), dims[axis_at] // blocks).reshape((-1,) + (1,) * (len(dims) - axis_at - 1))

    loudness = one(*cuts[0])
    for cut in cuts[1:]:
        loudness = loudness * one(*cut)
    return loudness


def scatter_about(stream_key, dims, deviation, most, shards=(), dtype=jnp.bfloat16):
    drawn = deviation * jax.random.normal(stream_key, dims, jnp.float32)
    if shards:
        drawn = drawn * level_of(stream_key, dims, shards, -0.22, 0.18)
    return jnp.clip(drawn, -most, most).astype(dtype)


def setup_inputs(seed: int = 0) -> dict:
    key_of = jax.random.split(jax.random.key(seed), 5)
    return {
        "start_states": draw_start_states(jax.random.fold_in(key_of[4], 71), 0),
        "bathymetry": jnp.clip(jnp.exp(math.log(2.0) - 1.3862944 * jax.random.uniform(key_of[1], (NX, NY), jnp.float32) ** level_of(key_of[1], (NX, NY), ((0, 16),), -0.2, 0.2)), 0.5, 2.0),
        "forcing_amp": scatter_about(key_of[2], (NX, NY), 0.5, 3.0, ((0, 16),), jnp.float32),
        "land_mask": place_ends((jax.random.randint(key_of[3], (NX, NY), 0, 8) < 1).astype(jnp.int32), jax.random.fold_in(key_of[3], 1), 0, 1),
    }


TIME_STEP = 0.4
GRAVITY = 1.0
CORIOLIS = 0.3
FRICTION = 0.05
EPSILON = 1e-06

def across_cols(field):
    widths = [(0, 0)] * (field.ndim - 1) + [(1, 1)]
    padded = jnp.pad(field, widths)
    return (padded[..., 2:] - padded[..., :-2]) * 0.5

def momentum(height_rows, height, east_flow, north_flow, wet_cells, push):
    east_slope = (height_rows[..., 2:, :] - height_rows[..., :-2, :]) * 0.5
    north_slope = across_cols(height)
    east_next = wet_cells * (east_flow + TIME_STEP * (-GRAVITY * east_slope + CORIOLIS * north_flow - FRICTION * east_flow + push))
    north_next = wet_cells * (north_flow + TIME_STEP * (-GRAVITY * north_slope - CORIOLIS * east_flow - FRICTION * north_flow))
    return (east_next, north_next)

def continuity(height, flux_rows, north_flux, wet_cells):
    divergence = (flux_rows[..., 2:, :] - flux_rows[..., :-2, :]) * 0.5 + across_cols(north_flux)
    return height - TIME_STEP * wet_cells * divergence

def inner_sum(left, right):
    return jnp.sum(left * right)

def least_squares(hessenberg, start_norm):
    normal_matrix = jnp.dot(hessenberg.T, hessenberg, precision=lax.Precision.HIGHEST)
    right_side = start_norm * hessenberg[0]
    lower = jnp.linalg.cholesky(normal_matrix)
    forward = []
    for line in range(KRY):
        accum = right_side[line]
        for other in range(line):
            accum = accum - lower[line, other] * forward[other]
        forward.append(accum / lower[line, line])
    weights = list(forward)
    for line in reversed(range(KRY)):
        accum = forward[line]
        for other in range(line + 1, KRY):
            accum = accum - lower[other, line] * weights[other]
        weights[line] = accum / lower[line, line]
    return weights

def pad_rows(field):
    return jnp.pad(field, ((0, 0), (1, 1), (0, 0)))

def time_step(state, tide_cos, bathymetry, wet_cells, forcing_amp):
    height = state[:, 0]
    east_flow = state[:, 1]
    north_flow = state[:, 2]
    push = forcing_amp * tide_cos[:, None, None]
    east_next, north_next = momentum(pad_rows(height), height, east_flow, north_flow, wet_cells, push)
    total = bathymetry + height
    new_height = continuity(height, pad_rows(total * east_next), total * north_next, wet_cells)
    return jnp.stack([new_height, east_next, north_next], axis=1)

def defects(states, forcing_amp, bathymetry, wet_cells):
    order = jnp.arange(SEGS).astype(jnp.float32)
    ends = states
    for step in range(STEPS):
        tide_cos = jnp.cos(2.0 * math.pi * (order * STEPS + step) / (SEGS * STEPS))
        ends = time_step(ends, tide_cos, bathymetry, wet_cells, forcing_amp)
    return jnp.roll(ends, 1, axis=0) - states

def reference(start_states, bathymetry, forcing_amp, land_mask):
    wet_cells = (1 - land_mask).astype(jnp.float32)
    count = SEGS * 3 * NX * NY

    def residual_of(states_in):
        return defects(states_in, forcing_amp, bathymetry, wet_cells)
    states = start_states
    norms = []
    for newton in range(NEWTON):
        residual = residual_of(states)
        squares = inner_sum(residual, residual)
        norms.append(jnp.sqrt(squares / count))
        start_norm = jnp.sqrt(squares + EPSILON)
        basis = [-residual / start_norm]
        hessenberg = jnp.zeros((KRY + 1, KRY), jnp.float32)
        for column in range(KRY):
            image = jax.jvp(residual_of, (states,), (basis[column],))[1]
            projections = jnp.stack([inner_sum(image, vector) for vector in basis])
            for line in range(column + 1):
                image = image - projections[line] * basis[line]
            remainder = jnp.sqrt(inner_sum(image, image) + EPSILON)
            hessenberg = hessenberg.at[:column + 1, column].set(projections)
            hessenberg = hessenberg.at[column + 1, column].set(remainder)
            if column + 1 < KRY:
                basis.append(image / remainder)
        weights = least_squares(hessenberg, start_norm)
        for column in range(KRY):
            states = states + weights[column] * basis[column]
    residual = residual_of(states)
    norms.append(jnp.sqrt(inner_sum(residual, residual) / count))

    def objective(states_in, amp_in):
        gap = defects(states_in, amp_in, bathymetry, wet_cells)
        return 0.5 * inner_sum(gap, gap)
    grad_states, grad_amp = jax.grad(objective, argnums=(0, 1))(states, forcing_amp)
    return (states, grad_states, grad_amp, jnp.stack(norms))
```

```python
import math

import jax
import jax.numpy as jnp
from jax import lax
from jax.sharding import PartitionSpec as P

STEPS = 2
KRY = 3
NEWTON = 2


TIME_STEP = 0.4
GRAVITY = 1.0
CORIOLIS = 0.3
FRICTION = 0.05
EPSILON = 1e-06

HALO = 2 * STEPS


def across_cols(field):
    widths = [(0, 0)] * (field.ndim - 1) + [(1, 1)]
    padded = jnp.pad(field, widths)
    return (padded[..., 2:] - padded[..., :-2]) * 0.5


def pad_rows(field):
    widths = [(0, 0)] * (field.ndim - 2) + [(1, 1), (0, 0)]
    return jnp.pad(field, widths)


def momentum(height_rows, height, east_flow, north_flow, wet_cells, push):
    east_slope = (height_rows[..., 2:, :] - height_rows[..., :-2, :]) * 0.5
    north_slope = across_cols(height)
    east_next = wet_cells * (
        east_flow
        + TIME_STEP * (-GRAVITY * east_slope + CORIOLIS * north_flow - FRICTION * east_flow + push)
    )
    north_next = wet_cells * (
        north_flow
        + TIME_STEP * (-GRAVITY * north_slope - CORIOLIS * east_flow - FRICTION * north_flow)
    )
    return (east_next, north_next)


def continuity(height, flux_rows, north_flux, wet_cells):
    divergence = (flux_rows[..., 2:, :] - flux_rows[..., :-2, :]) * 0.5 + across_cols(north_flux)
    return height - TIME_STEP * wet_cells * divergence


def time_step(state, tide_cos, depth, wet, forcing):
    height = state[:, 0]
    east_flow = state[:, 1]
    north_flow = state[:, 2]
    push = forcing * tide_cos[:, None, None]
    east_next, north_next = momentum(pad_rows(height), height, east_flow, north_flow, wet, push)
    total = depth + height
    new_height = continuity(height, pad_rows(total * east_next), total * north_next, wet)
    return jnp.stack([new_height, east_next, north_next], axis=1)


def least_squares(hessenberg, start_norm):
    normal_matrix = jnp.dot(hessenberg.T, hessenberg, precision=lax.Precision.HIGHEST)
    right_side = start_norm * hessenberg[0]
    lower = jnp.linalg.cholesky(normal_matrix)
    forward = []
    for line in range(KRY):
        accum = right_side[line]
        for other in range(line):
            accum = accum - lower[line, other] * forward[other]
        forward.append(accum / lower[line, line])
    weights = list(forward)
    for line in reversed(range(KRY)):
        accum = forward[line]
        for other in range(line + 1, KRY):
            accum = accum - lower[other, line] * weights[other]
        weights[line] = accum / lower[line, line]
    return weights


def with_halo(array, dim):
    size, length = lax.axis_size("space"), array.shape[dim]
    down = [(i, i + 1) for i in range(size - 1)]
    up = [(i + 1, i) for i in range(size - 1)]
    last = lax.slice_in_dim(array, length - HALO, length, axis=dim)
    first = lax.slice_in_dim(array, 0, HALO, axis=dim)
    before = lax.ppermute(last, "space", down)
    after = lax.ppermute(first, "space", up)
    return jnp.concatenate([before, array, after], axis=dim)


def fold_halo(array, dim):
    size, length = lax.axis_size("space"), array.shape[dim]
    down = [(i, i + 1) for i in range(size - 1)]
    up = [(i + 1, i) for i in range(size - 1)]
    head = lax.slice_in_dim(array, 0, HALO, axis=dim)
    tail = lax.slice_in_dim(array, length - HALO, length, axis=dim)
    inside = lax.slice_in_dim(array, HALO, length - HALO, axis=dim)
    from_above = lax.ppermute(tail, "space", down)
    from_below = lax.ppermute(head, "space", up)
    rows = inside.shape[dim]
    zeros = jnp.zeros_like(lax.slice_in_dim(inside, 0, rows - 2 * HALO, axis=dim))
    return inside + jnp.concatenate([from_above, zeros, from_below], axis=dim)


def tm_pairs(steps):
    count = lax.axis_size("tm")
    return [(source, (source + steps) % count) for source in range(count)]


def diagonal_pairs(row_step):
    ntm, nsp = lax.axis_size("tm"), lax.axis_size("space")
    pairs = []
    for t in range(ntm):
        for s in range(nsp):
            if 0 <= s + row_step < nsp:
                pairs.append((t * nsp + s, ((t + 1) % ntm) * nsp + s + row_step))
    return pairs


def ahead(segments):
    incoming = lax.ppermute(segments[-1:], "tm", tm_pairs(1))
    return jnp.concatenate([incoming, segments[:-1]], axis=0)


def behind(segments):
    incoming = lax.ppermute(segments[:1], "tm", tm_pairs(-1))
    return jnp.concatenate([segments[1:], incoming], axis=0)


def ahead_wide(segments):
    length = segments.shape[2]
    last = segments[-1:]
    inside = jnp.concatenate([lax.ppermute(last, "tm", tm_pairs(1)), segments[:-1]], axis=0)
    top = lax.ppermute(last[:, :, length - HALO :], ("tm", "space"), diagonal_pairs(1))
    bottom = lax.ppermute(last[:, :, :HALO], ("tm", "space"), diagonal_pairs(-1))
    if segments.shape[0] > 1:
        nsp = lax.axis_size("space")
        rest = segments[:-1]
        top_rest = lax.ppermute(rest[:, :, length - HALO :], "space", [(i, i + 1) for i in range(nsp - 1)])
        bottom_rest = lax.ppermute(rest[:, :, :HALO], "space", [(i + 1, i) for i in range(nsp - 1)])
        top = jnp.concatenate([top, top_rest], axis=0)
        bottom = jnp.concatenate([bottom, bottom_rest], axis=0)
    return jnp.concatenate([top, inside, bottom], axis=2)


def global_sum(value):
    ntm, nsp = lax.axis_size("tm"), lax.axis_size("space")
    for axis, size in (("space", nsp), ("tm", ntm)):
        if size & (size - 1):
            value = lax.psum(value, axis)
            continue
        step = 1
        while step < size:
            value = value + lax.ppermute(value, axis, [(i, i ^ step) for i in range(size)])
            step *= 2
    return value


def sum_scatter_tm(value, dim):
    size = lax.axis_size("tm")
    if size & (size - 1):
        return lax.psum_scatter(value, "tm", scatter_dimension=dim, tiled=True)
    index = lax.axis_index("tm")
    step = size // 2
    while step >= 1:
        half = value.shape[dim] // 2
        low = lax.slice_in_dim(value, 0, half, axis=dim)
        high = lax.slice_in_dim(value, half, 2 * half, axis=dim)
        upper = (index // step) % 2 == 1
        keep = jnp.where(upper, high, low)
        give = jnp.where(upper, low, high)
        value = keep + lax.ppermute(give, "tm", [(i, i ^ step) for i in range(size)])
        step //= 2
    return value


def quad(left, gram, right):
    return jnp.sum(left[:, None] * gram * right[None, :])


def krylov_combination(gram, start_norm):
    size = KRY + 1
    unit = jnp.zeros((size,), jnp.float32).at[0].set(1.0)
    basis = [-unit / start_norm]
    hessenberg = jnp.zeros((KRY + 1, KRY), jnp.float32)
    for column in range(KRY):
        image = jnp.concatenate([jnp.zeros((1,), jnp.float32), basis[column][:-1]])
        projections = jnp.stack([quad(image, gram, vector) for vector in basis])
        for line in range(column + 1):
            image = image - projections[line] * basis[line]
        remainder = jnp.sqrt(quad(image, gram, image) + EPSILON)
        hessenberg = hessenberg.at[: column + 1, column].set(projections)
        hessenberg = hessenberg.at[column + 1, column].set(remainder)
        if column + 1 < KRY:
            basis.append(image / remainder)
    weights = least_squares(hessenberg, start_norm)
    total = weights[0] * basis[0]
    for column in range(1, KRY):
        total = total + weights[column] * basis[column]
    return total


def per_device(start_states, bathymetry, forcing_amp, land_mask):
    seg_local, _, rows, cols = start_states.shape
    segs = seg_local * lax.axis_size("tm")
    count = segs * 3 * rows * lax.axis_size("space") * cols
    wet_cells = (1 - land_mask).astype(jnp.float32)
    order = (lax.axis_index("tm") * seg_local + jnp.arange(seg_local)).astype(jnp.float32)
    cosines = [
        jnp.cos(2.0 * math.pi * (order * STEPS + step) / (segs * STEPS)) for step in range(STEPS)
    ]

    both = jnp.concatenate(
        [jnp.stack([bathymetry, wet_cells, forcing_amp]), start_states.reshape(seg_local * 3, rows, cols)],
        axis=0,
    )
    both = with_halo(both, 1)
    depth_w, wet_w, forcing_w = both[0], both[1], both[2]
    states_w = both[3:].reshape(seg_local, 3, rows + 2 * HALO, cols)

    def interior(wide):
        return wide[:, :, HALO : HALO + rows]

    def run_forward(wide, forcing):
        for step in range(STEPS):
            wide = time_step(wide, cosines[step], depth_w, wet_w, forcing)
        return interior(wide)

    def advance(wide):
        return run_forward(wide, forcing_w)

    norms = []
    for newton in range(NEWTON):
        ends, tangent = jax.linearize(advance, states_w)
        krylov = [ahead_wide(ends) - states_w]
        for power in range(KRY):
            krylov.append(ahead_wide(tangent(krylov[-1])) - krylov[-1])
        inner = [interior(vector) for vector in krylov]
        local = []
        for a in range(KRY + 1):
            for b in range(a, KRY + 1):
                local.append(jnp.sum(inner[a] * inner[b]))
        totals = global_sum(jnp.stack(local))
        gram = [[None] * (KRY + 1) for _ in range(KRY + 1)]
        at = 0
        for a in range(KRY + 1):
            for b in range(a, KRY + 1):
                gram[a][b] = totals[at]
                gram[b][a] = totals[at]
                at += 1
        gram = jnp.stack([jnp.stack(line) for line in gram])
        squares = gram[0, 0]
        norms.append(jnp.sqrt(squares / count))
        start_norm = jnp.sqrt(squares + EPSILON)
        combination = krylov_combination(gram, start_norm)
        for a in range(KRY + 1):
            states_w = states_w + combination[a] * krylov[a]
    states = interior(states_w)
    following = behind(states)
    ends, back = jax.vjp(run_forward, states_w, forcing_w)
    residual = ahead(ends) - states
    squares = global_sum(jnp.sum(residual * residual))
    norms.append(jnp.sqrt(squares / count))
    cot_states, cot_amp = back(ends - following)
    width = rows + 2 * HALO
    folded = fold_halo(
        jnp.concatenate([cot_states.reshape(seg_local * 3, width, cols), cot_amp[None]], axis=0), 1
    )
    grad_states = folded[: seg_local * 3].reshape(seg_local, 3, rows, cols) - residual
    grad_amp = sum_scatter_tm(folded[seg_local * 3], 1)
    return (states, grad_states, grad_amp, jnp.stack(norms))


def solution(mesh):
    placed = (P("tm", None, "space", None), P("space", None), P("space", None), P("space", None))
    return jax.shard_map(
        per_device,
        mesh=mesh,
        in_specs=placed,
        out_specs=(
            P("tm", None, "space", None),
            P("tm", None, "space", None),
            P("space", "tm"),
            P(),
        ),
        check_vma=False,
    )
```

```python
import math

import jax
import jax.numpy as jnp
from jax import lax
from jax.sharding import PartitionSpec as P

STEPS = 2
KRY = 3
NEWTON = 2


TIME_STEP = 0.4
GRAVITY = 1.0
CORIOLIS = 0.3
FRICTION = 0.05
EPSILON = 1e-06

HALO = 2 * STEPS


def across_cols(field):
    widths = [(0, 0)] * (field.ndim - 1) + [(1, 1)]
    padded = jnp.pad(field, widths)
    return (padded[..., 2:] - padded[..., :-2]) * 0.5


def pad_rows(field):
    widths = [(0, 0)] * (field.ndim - 2) + [(1, 1), (0, 0)]
    return jnp.pad(field, widths)


def momentum(height_rows, height, east_flow, north_flow, wet_cells, push):
    east_slope = (height_rows[..., 2:, :] - height_rows[..., :-2, :]) * 0.5
    north_slope = across_cols(height)
    east_next = wet_cells * (
        east_flow
        + TIME_STEP * (-GRAVITY * east_slope + CORIOLIS * north_flow - FRICTION * east_flow + push)
    )
    north_next = wet_cells * (
        north_flow
        + TIME_STEP * (-GRAVITY * north_slope - CORIOLIS * east_flow - FRICTION * north_flow)
    )
    return (east_next, north_next)


def continuity(height, flux_rows, north_flux, wet_cells):
    divergence = (flux_rows[..., 2:, :] - flux_rows[..., :-2, :]) * 0.5 + across_cols(north_flux)
    return height - TIME_STEP * wet_cells * divergence


def time_step(state, tide_cos, depth, wet, forcing):
    height = state[:, 0]
    east_flow = state[:, 1]
    north_flow = state[:, 2]
    push = forcing * tide_cos[:, None, None]
    east_next, north_next = momentum(pad_rows(height), height, east_flow, north_flow, wet, push)
    total = depth + height
    new_height = continuity(height, pad_rows(total * east_next), total * north_next, wet)
    return jnp.stack([new_height, east_next, north_next], axis=1)


def with_halo(array, dim):
    size, length = lax.axis_size("space"), array.shape[dim]
    down = [(i, i + 1) for i in range(size - 1)]
    up = [(i + 1, i) for i in range(size - 1)]
    last = lax.slice_in_dim(array, length - HALO, length, axis=dim)
    first = lax.slice_in_dim(array, 0, HALO, axis=dim)
    before = lax.ppermute(last, "space", down)
    after = lax.ppermute(first, "space", up)
    return jnp.concatenate([before, array, after], axis=dim)


def fold_halo(array, dim):
    size, length = lax.axis_size("space"), array.shape[dim]
    down = [(i, i + 1) for i in range(size - 1)]
    up = [(i + 1, i) for i in range(size - 1)]
    head = lax.slice_in_dim(array, 0, HALO, axis=dim)
    tail = lax.slice_in_dim(array, length - HALO, length, axis=dim)
    inside = lax.slice_in_dim(array, HALO, length - HALO, axis=dim)
    from_above = lax.ppermute(tail, "space", down)
    from_below = lax.ppermute(head, "space", up)
    rows = inside.shape[dim]
    zeros = jnp.zeros_like(lax.slice_in_dim(inside, 0, rows - 2 * HALO, axis=dim))
    return inside + jnp.concatenate([from_above, zeros, from_below], axis=dim)


def tm_pairs(steps):
    count = lax.axis_size("tm")
    return [(source, (source + steps) % count) for source in range(count)]


def diagonal_pairs(row_step):
    ntm, nsp = lax.axis_size("tm"), lax.axis_size("space")
    pairs = []
    for t in range(ntm):
        for s in range(nsp):
            if 0 <= s + row_step < nsp:
                pairs.append((t * nsp + s, ((t + 1) % ntm) * nsp + s + row_step))
    return pairs


def ahead(segments):
    incoming = lax.ppermute(segments[-1:], "tm", tm_pairs(1))
    return jnp.concatenate([incoming, segments[:-1]], axis=0)


def behind(segments):
    incoming = lax.ppermute(segments[:1], "tm", tm_pairs(-1))
    return jnp.concatenate([segments[1:], incoming], axis=0)


def ahead_wide(segments):
    length = segments.shape[2]
    last = segments[-1:]
    inside = jnp.concatenate([lax.ppermute(last, "tm", tm_pairs(1)), segments[:-1]], axis=0)
    top = lax.ppermute(last[:, :, length - HALO :], ("tm", "space"), diagonal_pairs(1))
    bottom = lax.ppermute(last[:, :, :HALO], ("tm", "space"), diagonal_pairs(-1))
    if segments.shape[0] > 1:
        nsp = lax.axis_size("space")
        rest = segments[:-1]
        top_rest = lax.ppermute(rest[:, :, length - HALO :], "space", [(i, i + 1) for i in range(nsp - 1)])
        bottom_rest = lax.ppermute(rest[:, :, :HALO], "space", [(i + 1, i) for i in range(nsp - 1)])
        top = jnp.concatenate([top, top_rest], axis=0)
        bottom = jnp.concatenate([bottom, bottom_rest], axis=0)
    return jnp.concatenate([top, inside, bottom], axis=2)


def global_sum(value):
    ntm, nsp = lax.axis_size("tm"), lax.axis_size("space")
    for axis, size in (("space", nsp), ("tm", ntm)):
        if size & (size - 1):
            value = lax.psum(value, axis)
            continue
        step = 1
        while step < size:
            value = value + lax.ppermute(value, axis, [(i, i ^ step) for i in range(size)])
            step *= 2
    return value


def sum_over(value, axis):
    size = lax.axis_size(axis)
    if size & (size - 1):
        return lax.psum(value, axis)
    step = 1
    while step < size:
        value = value + lax.ppermute(value, axis, [(i, i ^ step) for i in range(size)])
        step *= 2
    return value


def sum_scatter_tm(value, rider):
    size = lax.axis_size("tm")
    if size & (size - 1):
        return lax.psum_scatter(value, "tm", scatter_dimension=1, tiled=True), lax.psum(rider, "tm")
    index = lax.axis_index("tm")
    lanes = 128
    step = size // 2
    while step >= 1:
        half = value.shape[1] // 2
        low = value[:, :half]
        high = value[:, half:]
        upper = (index // step) % 2 == 1
        keep = jnp.where(upper, high, low)
        give = jnp.where(upper, low, high)
        packed = jnp.concatenate([give, jnp.broadcast_to(rider, (value.shape[0], lanes))], axis=1)
        got = lax.ppermute(packed, "tm", [(i, i ^ step) for i in range(size)])
        value = keep + got[:, :half]
        rider = rider + got[0, half]
        step //= 2
    return value, rider


def quad(left, gram, right):
    total = None
    for a, lv in enumerate(left):
        if lv is None:
            continue
        for b, rv in enumerate(right):
            if rv is None:
                continue
            term = lv * gram[a][b] * rv
            total = term if total is None else total + term
    return total


def cholesky_solve(hessenberg, start_norm):
    normal = [[None] * KRY for _ in range(KRY)]
    for i in range(KRY):
        for j in range(i + 1):
            acc = None
            for k in range(KRY + 1):
                if hessenberg[k][i] is None or hessenberg[k][j] is None:
                    continue
                term = hessenberg[k][i] * hessenberg[k][j]
                acc = term if acc is None else acc + term
            normal[i][j] = acc
    lower = [[None] * KRY for _ in range(KRY)]
    for j in range(KRY):
        acc = normal[j][j]
        for k in range(j):
            acc = acc - lower[j][k] * lower[j][k]
        lower[j][j] = jnp.sqrt(acc)
        for i in range(j + 1, KRY):
            acc = normal[i][j]
            for k in range(j):
                acc = acc - lower[i][k] * lower[j][k]
            lower[i][j] = acc / lower[j][j]
    right_side = [start_norm * hessenberg[0][j] for j in range(KRY)]
    forward = []
    for line in range(KRY):
        accum = right_side[line]
        for other in range(line):
            accum = accum - lower[line][other] * forward[other]
        forward.append(accum / lower[line][line])
    weights = list(forward)
    for line in reversed(range(KRY)):
        accum = forward[line]
        for other in range(line + 1, KRY):
            accum = accum - lower[other][line] * weights[other]
        weights[line] = accum / lower[line][line]
    return weights


def krylov_combination(gram, start_norm):
    size = KRY + 1
    basis = [[-1.0 / start_norm] + [None] * (size - 1)]
    hessenberg = [[None] * KRY for _ in range(KRY + 1)]
    for column in range(KRY):
        image = [None] + basis[column][:-1]
        projections = [quad(image, gram, vector) for vector in basis]
        for line in range(column + 1):
            for a in range(size):
                if basis[line][a] is None:
                    continue
                part = projections[line] * basis[line][a]
                image[a] = -part if image[a] is None else image[a] - part
        remainder = jnp.sqrt(quad(image, gram, image) + EPSILON)
        for line in range(column + 1):
            hessenberg[line][column] = projections[line]
        hessenberg[column + 1][column] = remainder
        if column + 1 < KRY:
            basis.append([None if v is None else v / remainder for v in image])
    weights = cholesky_solve(hessenberg, start_norm)
    total = [None] * size
    for column in range(KRY):
        for a in range(size):
            if basis[column][a] is None:
                continue
            part = weights[column] * basis[column][a]
            total[a] = part if total[a] is None else total[a] + part
    return total


def per_device(start_states, bathymetry, forcing_amp, land_mask):
    seg_local, _, rows, cols = start_states.shape
    segs = seg_local * lax.axis_size("tm")
    count = segs * 3 * rows * lax.axis_size("space") * cols
    wet_cells = (1 - land_mask).astype(jnp.float32)
    order = (lax.axis_index("tm") * seg_local + jnp.arange(seg_local)).astype(jnp.float32)
    cosines = [
        jnp.cos(2.0 * math.pi * (order * STEPS + step) / (segs * STEPS)) for step in range(STEPS)
    ]

    both = jnp.concatenate(
        [jnp.stack([bathymetry, wet_cells, forcing_amp]), start_states.reshape(seg_local * 3, rows, cols)],
        axis=0,
    )
    both = with_halo(both, 1)
    depth_w, wet_w, forcing_w = both[0], both[1], both[2]
    states_w = both[3:].reshape(seg_local, 3, rows + 2 * HALO, cols)

    def interior(wide):
        return wide[:, :, HALO : HALO + rows]

    def run_forward(wide, forcing):
        for step in range(STEPS):
            wide = time_step(wide, cosines[step], depth_w, wet_w, forcing)
        return interior(wide)

    def advance(wide):
        return run_forward(wide, forcing_w)

    norms = []
    for newton in range(NEWTON):
        ends, tangent = jax.linearize(advance, states_w)
        krylov = [ahead_wide(ends) - states_w]
        for power in range(KRY):
            krylov.append(ahead_wide(tangent(krylov[-1])) - krylov[-1])
        inner = [interior(vector) for vector in krylov]
        local = []
        for a in range(KRY + 1):
            for b in range(a, KRY + 1):
                local.append(jnp.sum(inner[a] * inner[b]))
        totals = global_sum(jnp.stack(local))
        gram = [[None] * (KRY + 1) for _ in range(KRY + 1)]
        at = 0
        for a in range(KRY + 1):
            for b in range(a, KRY + 1):
                gram[a][b] = totals[at]
                gram[b][a] = totals[at]
                at += 1
        squares = gram[0][0]
        norms.append(jnp.sqrt(squares / count))
        start_norm = jnp.sqrt(squares + EPSILON)
        combination = krylov_combination(gram, start_norm)
        for a in range(KRY + 1):
            if combination[a] is not None:
                states_w = states_w + combination[a] * krylov[a]
    states = interior(states_w)
    following = behind(states)
    ends, back = jax.vjp(run_forward, states_w, forcing_w)
    residual = ahead(ends) - states
    squares = sum_over(jnp.sum(residual * residual), "space")
    cot_states, cot_amp = back(ends - following)
    width = rows + 2 * HALO
    folded = fold_halo(
        jnp.concatenate([cot_states.reshape(seg_local * 3, width, cols), cot_amp[None]], axis=0), 1
    )
    grad_states = folded[: seg_local * 3].reshape(seg_local, 3, rows, cols) - residual
    grad_amp, squares = sum_scatter_tm(folded[seg_local * 3], squares)
    norms.append(jnp.sqrt(squares / count))
    return (states, grad_states, grad_amp, jnp.stack(norms))


def solution(mesh):
    placed = (P("tm", None, "space", None), P("space", None), P("space", None), P("space", None))
    return jax.shard_map(
        per_device,
        mesh=mesh,
        in_specs=placed,
        out_specs=(
            P("tm", None, "space", None),
            P("tm", None, "space", None),
            P("space", "tm"),
            P(),
        ),
        check_vma=False,
    )
```

```python
import math

import jax
import jax.numpy as jnp
from jax import lax
from jax.sharding import PartitionSpec as P

STEPS = 2
KRY = 3
NEWTON = 2


TIME_STEP = 0.4
GRAVITY = 1.0
CORIOLIS = 0.3
FRICTION = 0.05
EPSILON = 1e-06

HALO = 2 * STEPS


def across_cols(field):
    widths = [(0, 0)] * (field.ndim - 1) + [(1, 1)]
    padded = jnp.pad(field, widths)
    return (padded[..., 2:] - padded[..., :-2]) * 0.5


def pad_rows(field):
    widths = [(0, 0)] * (field.ndim - 2) + [(1, 1), (0, 0)]
    return jnp.pad(field, widths)


def momentum(height_rows, height, east_flow, north_flow, wet_cells, push):
    east_slope = (height_rows[..., 2:, :] - height_rows[..., :-2, :]) * 0.5
    north_slope = across_cols(height)
    east_next = wet_cells * (
        east_flow
        + TIME_STEP * (-GRAVITY * east_slope + CORIOLIS * north_flow - FRICTION * east_flow + push)
    )
    north_next = wet_cells * (
        north_flow
        + TIME_STEP * (-GRAVITY * north_slope - CORIOLIS * east_flow - FRICTION * north_flow)
    )
    return (east_next, north_next)


def continuity(height, flux_rows, north_flux, wet_cells):
    divergence = (flux_rows[..., 2:, :] - flux_rows[..., :-2, :]) * 0.5 + across_cols(north_flux)
    return height - TIME_STEP * wet_cells * divergence


def time_step(state, tide_cos, depth, wet, forcing):
    height = state[:, 0]
    east_flow = state[:, 1]
    north_flow = state[:, 2]
    push = forcing * tide_cos[:, None, None]
    east_next, north_next = momentum(pad_rows(height), height, east_flow, north_flow, wet, push)
    total = depth + height
    new_height = continuity(height, pad_rows(total * east_next), total * north_next, wet)
    return jnp.stack([new_height, east_next, north_next], axis=1)


def with_halo(array, dim):
    size, length = lax.axis_size("space"), array.shape[dim]
    down = [(i, i + 1) for i in range(size - 1)]
    up = [(i + 1, i) for i in range(size - 1)]
    last = lax.slice_in_dim(array, length - HALO, length, axis=dim)
    first = lax.slice_in_dim(array, 0, HALO, axis=dim)
    before = lax.ppermute(last, "space", down)
    after = lax.ppermute(first, "space", up)
    return jnp.concatenate([before, array, after], axis=dim)


def fold_halo(array, dim):
    size, length = lax.axis_size("space"), array.shape[dim]
    down = [(i, i + 1) for i in range(size - 1)]
    up = [(i + 1, i) for i in range(size - 1)]
    head = lax.slice_in_dim(array, 0, HALO, axis=dim)
    tail = lax.slice_in_dim(array, length - HALO, length, axis=dim)
    inside = lax.slice_in_dim(array, HALO, length - HALO, axis=dim)
    from_above = lax.ppermute(tail, "space", down)
    from_below = lax.ppermute(head, "space", up)
    rows = inside.shape[dim]
    zeros = jnp.zeros_like(lax.slice_in_dim(inside, 0, rows - 2 * HALO, axis=dim))
    return inside + jnp.concatenate([from_above, zeros, from_below], axis=dim)


def tm_pairs(steps):
    count = lax.axis_size("tm")
    return [(source, (source + steps) % count) for source in range(count)]


def diagonal_pairs(row_step):
    ntm, nsp = lax.axis_size("tm"), lax.axis_size("space")
    pairs = []
    for t in range(ntm):
        for s in range(nsp):
            if 0 <= s + row_step < nsp:
                pairs.append((t * nsp + s, ((t + 1) % ntm) * nsp + s + row_step))
    return pairs


def ahead(segments):
    incoming = lax.ppermute(segments[-1:], "tm", tm_pairs(1))
    return jnp.concatenate([incoming, segments[:-1]], axis=0)


def behind(segments):
    incoming = lax.ppermute(segments[:1], "tm", tm_pairs(-1))
    return jnp.concatenate([segments[1:], incoming], axis=0)


def ahead_wide(segments):
    length = segments.shape[2]
    last = segments[-1:]
    inside = jnp.concatenate([lax.ppermute(last, "tm", tm_pairs(1)), segments[:-1]], axis=0)
    top = lax.ppermute(last[:, :, length - HALO :], ("tm", "space"), diagonal_pairs(1))
    bottom = lax.ppermute(last[:, :, :HALO], ("tm", "space"), diagonal_pairs(-1))
    if segments.shape[0] > 1:
        nsp = lax.axis_size("space")
        rest = segments[:-1]
        top_rest = lax.ppermute(rest[:, :, length - HALO :], "space", [(i, i + 1) for i in range(nsp - 1)])
        bottom_rest = lax.ppermute(rest[:, :, :HALO], "space", [(i + 1, i) for i in range(nsp - 1)])
        top = jnp.concatenate([top, top_rest], axis=0)
        bottom = jnp.concatenate([bottom, bottom_rest], axis=0)
    return jnp.concatenate([top, inside, bottom], axis=2)


def global_sum(value):
    ntm, nsp = lax.axis_size("tm"), lax.axis_size("space")
    for axis, size in (("space", nsp), ("tm", ntm)):
        if size & (size - 1):
            value = lax.psum(value, axis)
            continue
        step = 1
        while step < size:
            value = value + lax.ppermute(value, axis, [(i, i ^ step) for i in range(size)])
            step *= 2
    return value


def sum_over(value, axis):
    size = lax.axis_size(axis)
    if size & (size - 1):
        return lax.psum(value, axis)
    step = 1
    while step < size:
        value = value + lax.ppermute(value, axis, [(i, i ^ step) for i in range(size)])
        step *= 2
    return value


def sum_scatter_tm(value, rider):
    size = lax.axis_size("tm")
    if size & (size - 1):
        return lax.psum_scatter(value, "tm", scatter_dimension=1, tiled=True), lax.psum(rider, "tm")
    index = lax.axis_index("tm")
    lanes = 128
    step = size // 2
    while step >= 1:
        half = value.shape[1] // 2
        low = value[:, :half]
        high = value[:, half:]
        upper = (index // step) % 2 == 1
        keep = jnp.where(upper, high, low)
        give = jnp.where(upper, low, high)
        packed = jnp.concatenate([give, jnp.broadcast_to(rider, (value.shape[0], lanes))], axis=1)
        got = lax.ppermute(packed, "tm", [(i, i ^ step) for i in range(size)])
        value = keep + got[:, :half]
        rider = rider + got[0, half]
        step //= 2
    return value, rider


def quad(left, gram, right):
    total = None
    for a, lv in enumerate(left):
        if lv is None:
            continue
        for b, rv in enumerate(right):
            if rv is None:
                continue
            term = lv * gram[a][b] * rv
            total = term if total is None else total + term
    return total


def cholesky_solve(hessenberg, start_norm):
    normal = [[None] * KRY for _ in range(KRY)]
    for i in range(KRY):
        for j in range(i + 1):
            acc = None
            for k in range(KRY + 1):
                if hessenberg[k][i] is None or hessenberg[k][j] is None:
                    continue
                term = hessenberg[k][i] * hessenberg[k][j]
                acc = term if acc is None else acc + term
            normal[i][j] = acc
    lower = [[None] * KRY for _ in range(KRY)]
    for j in range(KRY):
        acc = normal[j][j]
        for k in range(j):
            acc = acc - lower[j][k] * lower[j][k]
        lower[j][j] = jnp.sqrt(acc)
        for i in range(j + 1, KRY):
            acc = normal[i][j]
            for k in range(j):
                acc = acc - lower[i][k] * lower[j][k]
            lower[i][j] = acc / lower[j][j]
    right_side = [start_norm * hessenberg[0][j] for j in range(KRY)]
    forward = []
    for line in range(KRY):
        accum = right_side[line]
        for other in range(line):
            accum = accum - lower[line][other] * forward[other]
        forward.append(accum / lower[line][line])
    weights = list(forward)
    for line in reversed(range(KRY)):
        accum = forward[line]
        for other in range(line + 1, KRY):
            accum = accum - lower[other][line] * weights[other]
        weights[line] = accum / lower[line][line]
    return weights


def krylov_combination(gram, start_norm):
    size = KRY + 1
    basis = [[-1.0 / start_norm] + [None] * (size - 1)]
    hessenberg = [[None] * KRY for _ in range(KRY + 1)]
    for column in range(KRY):
        image = [None] + basis[column][:-1]
        projections = [quad(image, gram, vector) for vector in basis]
        for line in range(column + 1):
            for a in range(size):
                if basis[line][a] is None:
                    continue
                part = projections[line] * basis[line][a]
                image[a] = -part if image[a] is None else image[a] - part
        remainder = jnp.sqrt(quad(image, gram, image) + EPSILON)
        for line in range(column + 1):
            hessenberg[line][column] = projections[line]
        hessenberg[column + 1][column] = remainder
        if column + 1 < KRY:
            basis.append([None if v is None else v / remainder for v in image])
    weights = cholesky_solve(hessenberg, start_norm)
    total = [None] * size
    for column in range(KRY):
        for a in range(size):
            if basis[column][a] is None:
                continue
            part = weights[column] * basis[column][a]
            total[a] = part if total[a] is None else total[a] + part
    return total


def per_device(start_states, bathymetry, forcing_amp, land_mask):
    seg_local, _, rows, cols = start_states.shape
    segs = seg_local * lax.axis_size("tm")
    count = segs * 3 * rows * lax.axis_size("space") * cols
    wet_cells = (1 - land_mask).astype(jnp.float32)
    order = (lax.axis_index("tm") * seg_local + jnp.arange(seg_local)).astype(jnp.float32)
    cosines = [
        jnp.cos(2.0 * math.pi * (order * STEPS + step) / (segs * STEPS)) for step in range(STEPS)
    ]

    both = jnp.concatenate(
        [jnp.stack([bathymetry, wet_cells, forcing_amp]), start_states.reshape(seg_local * 3, rows, cols)],
        axis=0,
    )
    both = with_halo(both, 1)
    depth_w, wet_w, forcing_w = both[0], both[1], both[2]
    states_w = both[3:].reshape(seg_local, 3, rows + 2 * HALO, cols)

    def interior(wide):
        return wide[:, :, HALO : HALO + rows]

    def run_forward(wide, forcing):
        for step in range(STEPS):
            wide = time_step(wide, cosines[step], depth_w, wet_w, forcing)
        return interior(wide)

    def advance(wide):
        return run_forward(wide, forcing_w)

    norms = []
    for newton in range(NEWTON):
        ends, tangent = jax.linearize(advance, states_w)
        krylov = [ahead_wide(ends) - states_w]
        for power in range(KRY):
            krylov.append(ahead_wide(tangent(krylov[-1])) - krylov[-1])
        flat = jnp.stack([interior(vector).reshape(-1) for vector in krylov])
        local = jnp.dot(flat, flat.T, precision=lax.Precision.HIGHEST)
        totals = global_sum(jnp.broadcast_to(local[:, :, None], local.shape + (128,)))
        gram = [[totals[a, b] for b in range(KRY + 1)] for a in range(KRY + 1)]
        squares = gram[0][0]
        norms.append(jnp.sqrt(squares[0] / count))
        start_norm = jnp.sqrt(squares + EPSILON)
        combination = krylov_combination(gram, start_norm)
        for a in range(KRY + 1):
            if combination[a] is not None:
                states_w = states_w + combination[a][0] * krylov[a]
    states = interior(states_w)
    following = behind(states)
    ends, back = jax.vjp(run_forward, states_w, forcing_w)
    residual = ahead(ends) - states
    squares = sum_over(jnp.sum(residual * residual), "space")
    cot_states, cot_amp = back(ends - following)
    width = rows + 2 * HALO
    folded = fold_halo(
        jnp.concatenate([cot_states.reshape(seg_local * 3, width, cols), cot_amp[None]], axis=0), 1
    )
    grad_states = folded[: seg_local * 3].reshape(seg_local, 3, rows, cols) - residual
    grad_amp, squares = sum_scatter_tm(folded[seg_local * 3], squares)
    norms.append(jnp.sqrt(squares / count))
    return (states, grad_states, grad_amp, jnp.stack(norms))


def solution(mesh):
    placed = (P("tm", None, "space", None), P("space", None), P("space", None), P("space", None))
    return jax.shard_map(
        per_device,
        mesh=mesh,
        in_specs=placed,
        out_specs=(
            P("tm", None, "space", None),
            P("tm", None, "space", None),
            P("space", "tm"),
            P(),
        ),
        check_vma=False,
    )
```

```python
import math

import jax
import jax.numpy as jnp
from jax import lax
from jax.sharding import PartitionSpec as P

STEPS = 2
KRY = 3
NEWTON = 2


TIME_STEP = 0.4
GRAVITY = 1.0
CORIOLIS = 0.3
FRICTION = 0.05
EPSILON = 1e-06

HALO = 2 * STEPS


def across_cols(field):
    widths = [(0, 0)] * (field.ndim - 1) + [(1, 1)]
    padded = jnp.pad(field, widths)
    return (padded[..., 2:] - padded[..., :-2]) * 0.5


def pad_rows(field):
    widths = [(0, 0)] * (field.ndim - 2) + [(1, 1), (0, 0)]
    return jnp.pad(field, widths)


def momentum(height_rows, height, east_flow, north_flow, wet_cells, push):
    east_slope = (height_rows[..., 2:, :] - height_rows[..., :-2, :]) * 0.5
    north_slope = across_cols(height)
    east_next = wet_cells * (
        east_flow
        + TIME_STEP * (-GRAVITY * east_slope + CORIOLIS * north_flow - FRICTION * east_flow + push)
    )
    north_next = wet_cells * (
        north_flow
        + TIME_STEP * (-GRAVITY * north_slope - CORIOLIS * east_flow - FRICTION * north_flow)
    )
    return (east_next, north_next)


def continuity(height, flux_rows, north_flux, wet_cells):
    divergence = (flux_rows[..., 2:, :] - flux_rows[..., :-2, :]) * 0.5 + across_cols(north_flux)
    return height - TIME_STEP * wet_cells * divergence


def time_step(state, tide_cos, depth, wet, forcing):
    height = state[:, 0]
    east_flow = state[:, 1]
    north_flow = state[:, 2]
    push = forcing * tide_cos[:, None, None]
    east_next, north_next = momentum(pad_rows(height), height, east_flow, north_flow, wet, push)
    total = depth + height
    new_height = continuity(height, pad_rows(total * east_next), total * north_next, wet)
    return jnp.stack([new_height, east_next, north_next], axis=1)


def with_halo(array, dim):
    size, length = lax.axis_size("space"), array.shape[dim]
    down = [(i, i + 1) for i in range(size - 1)]
    up = [(i + 1, i) for i in range(size - 1)]
    last = lax.slice_in_dim(array, length - HALO, length, axis=dim)
    first = lax.slice_in_dim(array, 0, HALO, axis=dim)
    before = lax.ppermute(last, "space", down)
    after = lax.ppermute(first, "space", up)
    return jnp.concatenate([before, array, after], axis=dim)


def fold_halo(array, dim):
    size, length = lax.axis_size("space"), array.shape[dim]
    down = [(i, i + 1) for i in range(size - 1)]
    up = [(i + 1, i) for i in range(size - 1)]
    head = lax.slice_in_dim(array, 0, HALO, axis=dim)
    tail = lax.slice_in_dim(array, length - HALO, length, axis=dim)
    inside = lax.slice_in_dim(array, HALO, length - HALO, axis=dim)
    from_above = lax.ppermute(tail, "space", down)
    from_below = lax.ppermute(head, "space", up)
    rows = inside.shape[dim]
    zeros = jnp.zeros_like(lax.slice_in_dim(inside, 0, rows - 2 * HALO, axis=dim))
    return inside + jnp.concatenate([from_above, zeros, from_below], axis=dim)


def tm_pairs(steps):
    count = lax.axis_size("tm")
    return [(source, (source + steps) % count) for source in range(count)]


def diagonal_pairs(row_step):
    ntm, nsp = lax.axis_size("tm"), lax.axis_size("space")
    pairs = []
    for t in range(ntm):
        for s in range(nsp):
            if 0 <= s + row_step < nsp:
                pairs.append((t * nsp + s, ((t + 1) % ntm) * nsp + s + row_step))
    return pairs


def ahead(segments):
    incoming = lax.ppermute(segments[-1:], "tm", tm_pairs(1))
    return jnp.concatenate([incoming, segments[:-1]], axis=0)


def behind(segments):
    incoming = lax.ppermute(segments[:1], "tm", tm_pairs(-1))
    return jnp.concatenate([segments[1:], incoming], axis=0)


def ahead_wide(segments):
    length = segments.shape[2]
    last = segments[-1:]
    inside = jnp.concatenate([lax.ppermute(last, "tm", tm_pairs(1)), segments[:-1]], axis=0)
    top = lax.ppermute(last[:, :, length - HALO :], ("tm", "space"), diagonal_pairs(1))
    bottom = lax.ppermute(last[:, :, :HALO], ("tm", "space"), diagonal_pairs(-1))
    if segments.shape[0] > 1:
        nsp = lax.axis_size("space")
        rest = segments[:-1]
        top_rest = lax.ppermute(rest[:, :, length - HALO :], "space", [(i, i + 1) for i in range(nsp - 1)])
        bottom_rest = lax.ppermute(rest[:, :, :HALO], "space", [(i + 1, i) for i in range(nsp - 1)])
        top = jnp.concatenate([top, top_rest], axis=0)
        bottom = jnp.concatenate([bottom, bottom_rest], axis=0)
    return jnp.concatenate([top, inside, bottom], axis=2)


def global_sum(value):
    ntm, nsp = lax.axis_size("tm"), lax.axis_size("space")
    for axis, size in (("space", nsp), ("tm", ntm)):
        if size & (size - 1):
            value = lax.psum(value, axis)
            continue
        step = 1
        while step < size:
            value = value + lax.ppermute(value, axis, [(i, i ^ step) for i in range(size)])
            step *= 2
    return value


def sum_over(value, axis):
    size = lax.axis_size(axis)
    if size & (size - 1):
        return lax.psum(value, axis)
    step = 1
    while step < size:
        value = value + lax.ppermute(value, axis, [(i, i ^ step) for i in range(size)])
        step *= 2
    return value


def sum_scatter_tm(value, rider):
    size = lax.axis_size("tm")
    if size & (size - 1):
        return lax.psum_scatter(value, "tm", scatter_dimension=1, tiled=True), lax.psum(rider, "tm")
    index = lax.axis_index("tm")
    lanes = 128
    step = size // 2
    while step >= 1:
        half = value.shape[1] // 2
        low = value[:, :half]
        high = value[:, half:]
        upper = (index // step) % 2 == 1
        keep = jnp.where(upper, high, low)
        give = jnp.where(upper, low, high)
        packed = jnp.concatenate([give, jnp.broadcast_to(rider, (value.shape[0], lanes))], axis=1)
        got = lax.ppermute(packed, "tm", [(i, i ^ step) for i in range(size)])
        value = keep + got[:, :half]
        rider = rider + got[0, half]
        step //= 2
    return value, rider


def quad(left, gram, right):
    total = None
    for a, lv in enumerate(left):
        if lv is None:
            continue
        for b, rv in enumerate(right):
            if rv is None:
                continue
            term = lv * gram[a][b] * rv
            total = term if total is None else total + term
    return total


def cholesky_solve(hessenberg, start_norm):
    normal = [[None] * KRY for _ in range(KRY)]
    for i in range(KRY):
        for j in range(i + 1):
            acc = None
            for k in range(KRY + 1):
                if hessenberg[k][i] is None or hessenberg[k][j] is None:
                    continue
                term = hessenberg[k][i] * hessenberg[k][j]
                acc = term if acc is None else acc + term
            normal[i][j] = acc
    lower = [[None] * KRY for _ in range(KRY)]
    for j in range(KRY):
        acc = normal[j][j]
        for k in range(j):
            acc = acc - lower[j][k] * lower[j][k]
        lower[j][j] = jnp.sqrt(acc)
        for i in range(j + 1, KRY):
            acc = normal[i][j]
            for k in range(j):
                acc = acc - lower[i][k] * lower[j][k]
            lower[i][j] = acc / lower[j][j]
    right_side = [start_norm * hessenberg[0][j] for j in range(KRY)]
    forward = []
    for line in range(KRY):
        accum = right_side[line]
        for other in range(line):
            accum = accum - lower[line][other] * forward[other]
        forward.append(accum / lower[line][line])
    weights = list(forward)
    for line in reversed(range(KRY)):
        accum = forward[line]
        for other in range(line + 1, KRY):
            accum = accum - lower[other][line] * weights[other]
        weights[line] = accum / lower[line][line]
    return weights


def krylov_combination(gram, start_norm):
    size = KRY + 1
    basis = [[-1.0 / start_norm] + [None] * (size - 1)]
    hessenberg = [[None] * KRY for _ in range(KRY + 1)]
    for column in range(KRY):
        image = [None] + basis[column][:-1]
        projections = [quad(image, gram, vector) for vector in basis]
        for line in range(column + 1):
            for a in range(size):
                if basis[line][a] is None:
                    continue
                part = projections[line] * basis[line][a]
                image[a] = -part if image[a] is None else image[a] - part
        remainder = jnp.sqrt(quad(image, gram, image) + EPSILON)
        for line in range(column + 1):
            hessenberg[line][column] = projections[line]
        hessenberg[column + 1][column] = remainder
        if column + 1 < KRY:
            basis.append([None if v is None else v / remainder for v in image])
    weights = cholesky_solve(hessenberg, start_norm)
    total = [None] * size
    for column in range(KRY):
        for a in range(size):
            if basis[column][a] is None:
                continue
            part = weights[column] * basis[column][a]
            total[a] = part if total[a] is None else total[a] + part
    return total


def per_device(start_states, bathymetry, forcing_amp, land_mask):
    seg_local, _, rows, cols = start_states.shape
    segs = seg_local * lax.axis_size("tm")
    count = segs * 3 * rows * lax.axis_size("space") * cols
    wet_cells = (1 - land_mask).astype(jnp.float32)
    order = (lax.axis_index("tm") * seg_local + jnp.arange(seg_local)).astype(jnp.float32)
    cosines = [
        jnp.cos(2.0 * math.pi * (order * STEPS + step) / (segs * STEPS)) for step in range(STEPS)
    ]

    both = jnp.concatenate(
        [jnp.stack([bathymetry, wet_cells, forcing_amp]), start_states.reshape(seg_local * 3, rows, cols)],
        axis=0,
    )
    both = with_halo(both, 1)
    depth_w, wet_w, forcing_w = both[0], both[1], both[2]
    states_w = both[3:].reshape(seg_local, 3, rows + 2 * HALO, cols)

    def interior(wide):
        return wide[:, :, HALO : HALO + rows]

    def run_forward(wide, forcing):
        for step in range(STEPS):
            wide = time_step(wide, cosines[step], depth_w, wet_w, forcing)
        return interior(wide)

    def advance(wide):
        return run_forward(wide, forcing_w)

    following = behind(start_states)
    norms = []
    for newton in range(NEWTON):
        ends, tangent = jax.linearize(advance, states_w)
        krylov = [ahead_wide(ends) - states_w]
        shifted = [ends - following]
        for power in range(KRY):
            image = tangent(krylov[-1])
            shifted.append(image - shifted[-1])
            if power + 1 < KRY:
                krylov.append(ahead_wide(image) - krylov[-1])
        flat = jnp.stack([vector.reshape(-1) for vector in shifted])
        local = jnp.dot(flat, flat.T, precision=lax.Precision.HIGHEST)
        totals = global_sum(jnp.broadcast_to(local[:, :, None], local.shape + (128,)))
        krylov.append(ahead_wide(image) - krylov[-1])
        gram = [[totals[a, b] for b in range(KRY + 1)] for a in range(KRY + 1)]
        squares = gram[0][0]
        norms.append(jnp.sqrt(squares[0] / count))
        start_norm = jnp.sqrt(squares + EPSILON)
        combination = krylov_combination(gram, start_norm)
        for a in range(KRY + 1):
            if combination[a] is not None:
                states_w = states_w + combination[a][0] * krylov[a]
                following = following + combination[a][0] * shifted[a]
    states = interior(states_w)
    ends, back = jax.vjp(run_forward, states_w, forcing_w)
    cotangent = ends - following
    squares = sum_over(jnp.sum(cotangent * cotangent), "space")
    residual = ahead(ends) - states
    cot_states, cot_amp = back(cotangent)
    width = rows + 2 * HALO
    folded = fold_halo(
        jnp.concatenate([cot_states.reshape(seg_local * 3, width, cols), cot_amp[None]], axis=0), 1
    )
    grad_states = folded[: seg_local * 3].reshape(seg_local, 3, rows, cols) - residual
    grad_amp, squares = sum_scatter_tm(folded[seg_local * 3], squares)
    norms.append(jnp.sqrt(squares / count))
    return (states, grad_states, grad_amp, jnp.stack(norms))


def solution(mesh):
    placed = (P("tm", None, "space", None), P("space", None), P("space", None), P("space", None))
    return jax.shard_map(
        per_device,
        mesh=mesh,
        in_specs=placed,
        out_specs=(
            P("tm", None, "space", None),
            P("tm", None, "space", None),
            P("space", "tm"),
            P(),
        ),
        check_vma=False,
    )
```

```python
import math

import jax
import jax.numpy as jnp
from jax import lax
from jax.sharding import PartitionSpec as P

STEPS = 2
KRY = 3
NEWTON = 2


TIME_STEP = 0.4
GRAVITY = 1.0
CORIOLIS = 0.3
FRICTION = 0.05
EPSILON = 1e-06

HALO = 2 * STEPS


def across_cols(field):
    widths = [(0, 0)] * (field.ndim - 1) + [(1, 1)]
    padded = jnp.pad(field, widths)
    return (padded[..., 2:] - padded[..., :-2]) * 0.5


def pad_rows(field):
    widths = [(0, 0)] * (field.ndim - 2) + [(1, 1), (0, 0)]
    return jnp.pad(field, widths)


def momentum(height_rows, height, east_flow, north_flow, wet_cells, push):
    east_slope = (height_rows[..., 2:, :] - height_rows[..., :-2, :]) * 0.5
    north_slope = across_cols(height)
    east_next = wet_cells * (
        east_flow
        + TIME_STEP * (-GRAVITY * east_slope + CORIOLIS * north_flow - FRICTION * east_flow + push)
    )
    north_next = wet_cells * (
        north_flow
        + TIME_STEP * (-GRAVITY * north_slope - CORIOLIS * east_flow - FRICTION * north_flow)
    )
    return (east_next, north_next)


def continuity(height, flux_rows, north_flux, wet_cells):
    divergence = (flux_rows[..., 2:, :] - flux_rows[..., :-2, :]) * 0.5 + across_cols(north_flux)
    return height - TIME_STEP * wet_cells * divergence


def time_step(state, tide_cos, depth, wet, forcing):
    height = state[:, 0]
    east_flow = state[:, 1]
    north_flow = state[:, 2]
    push = forcing * tide_cos[:, None, None]
    east_next, north_next = momentum(pad_rows(height), height, east_flow, north_flow, wet, push)
    total = depth + height
    new_height = continuity(height, pad_rows(total * east_next), total * north_next, wet)
    return jnp.stack([new_height, east_next, north_next], axis=1)


def with_halo(array, dim):
    size, length = lax.axis_size("space"), array.shape[dim]
    down = [(i, i + 1) for i in range(size - 1)]
    up = [(i + 1, i) for i in range(size - 1)]
    last = lax.slice_in_dim(array, length - HALO, length, axis=dim)
    first = lax.slice_in_dim(array, 0, HALO, axis=dim)
    before = lax.ppermute(last, "space", down)
    after = lax.ppermute(first, "space", up)
    return jnp.concatenate([before, array, after], axis=dim)


def fold_halo(array, dim):
    size, length = lax.axis_size("space"), array.shape[dim]
    down = [(i, i + 1) for i in range(size - 1)]
    up = [(i + 1, i) for i in range(size - 1)]
    head = lax.slice_in_dim(array, 0, HALO, axis=dim)
    tail = lax.slice_in_dim(array, length - HALO, length, axis=dim)
    inside = lax.slice_in_dim(array, HALO, length - HALO, axis=dim)
    from_above = lax.ppermute(tail, "space", down)
    from_below = lax.ppermute(head, "space", up)
    rows = inside.shape[dim]
    zeros = jnp.zeros_like(lax.slice_in_dim(inside, 0, rows - 2 * HALO, axis=dim))
    return inside + jnp.concatenate([from_above, zeros, from_below], axis=dim)


def tm_pairs(steps):
    count = lax.axis_size("tm")
    return [(source, (source + steps) % count) for source in range(count)]


def diagonal_pairs(row_step):
    ntm, nsp = lax.axis_size("tm"), lax.axis_size("space")
    pairs = []
    for t in range(ntm):
        for s in range(nsp):
            if 0 <= s + row_step < nsp:
                pairs.append((t * nsp + s, ((t + 1) % ntm) * nsp + s + row_step))
    return pairs


def ahead(segments):
    incoming = lax.ppermute(segments[-1:], "tm", tm_pairs(1))
    return jnp.concatenate([incoming, segments[:-1]], axis=0)


def behind(segments):
    incoming = lax.ppermute(segments[:1], "tm", tm_pairs(-1))
    return jnp.concatenate([segments[1:], incoming], axis=0)


def ahead_wide(segments):
    length = segments.shape[2]
    last = segments[-1:]
    inside = jnp.concatenate([lax.ppermute(last, "tm", tm_pairs(1)), segments[:-1]], axis=0)
    top = lax.ppermute(last[:, :, length - HALO :], ("tm", "space"), diagonal_pairs(1))
    bottom = lax.ppermute(last[:, :, :HALO], ("tm", "space"), diagonal_pairs(-1))
    if segments.shape[0] > 1:
        nsp = lax.axis_size("space")
        rest = segments[:-1]
        top_rest = lax.ppermute(rest[:, :, length - HALO :], "space", [(i, i + 1) for i in range(nsp - 1)])
        bottom_rest = lax.ppermute(rest[:, :, :HALO], "space", [(i + 1, i) for i in range(nsp - 1)])
        top = jnp.concatenate([top, top_rest], axis=0)
        bottom = jnp.concatenate([bottom, bottom_rest], axis=0)
    return jnp.concatenate([top, inside, bottom], axis=2)


def global_sum(value):
    ntm, nsp = lax.axis_size("tm"), lax.axis_size("space")
    for axis, size in (("space", nsp), ("tm", ntm)):
        if size & (size - 1):
            value = lax.psum(value, axis)
            continue
        step = 1
        while step < size:
            value = value + lax.ppermute(value, axis, [(i, i ^ step) for i in range(size)])
            step *= 2
    return value


def sum_over(value, axis):
    size = lax.axis_size(axis)
    if size & (size - 1):
        return lax.psum(value, axis)
    step = 1
    while step < size:
        value = value + lax.ppermute(value, axis, [(i, i ^ step) for i in range(size)])
        step *= 2
    return value


def sum_scatter_tm(value, rider):
    size = lax.axis_size("tm")
    rows, length = value.shape
    lanes = length // size
    if size & (size - 1) or lanes % 128:
        return lax.psum_scatter(value, "tm", scatter_dimension=1, tiled=True), lax.psum(rider, "tm")
    index = lax.axis_index("tm")
    blocks = value.reshape(rows, size, lanes)
    step = 1
    while step < size:
        pairs = blocks.reshape(rows, blocks.shape[1] // 2, 2, lanes)
        upper = (index // step) % 2 == 1
        keep = jnp.where(upper, pairs[:, :, 1], pairs[:, :, 0])
        give = jnp.where(upper, pairs[:, :, 0], pairs[:, :, 1])
        packed = jnp.concatenate([give, jnp.broadcast_to(rider, (rows, 1, lanes))], axis=1)
        got = lax.ppermute(packed, "tm", [(i, i ^ step) for i in range(size)])
        blocks = keep + got[:, :-1]
        rider = rider + got[0, -1, 0]
        step *= 2
    return blocks.reshape(rows, lanes), rider


def quad(left, gram, right):
    total = None
    for a, lv in enumerate(left):
        if lv is None:
            continue
        for b, rv in enumerate(right):
            if rv is None:
                continue
            term = lv * gram[a][b] * rv
            total = term if total is None else total + term
    return total


def cholesky_solve(hessenberg, start_norm):
    normal = [[None] * KRY for _ in range(KRY)]
    for i in range(KRY):
        for j in range(i + 1):
            acc = None
            for k in range(KRY + 1):
                if hessenberg[k][i] is None or hessenberg[k][j] is None:
                    continue
                term = hessenberg[k][i] * hessenberg[k][j]
                acc = term if acc is None else acc + term
            normal[i][j] = acc
    lower = [[None] * KRY for _ in range(KRY)]
    for j in range(KRY):
        acc = normal[j][j]
        for k in range(j):
            acc = acc - lower[j][k] * lower[j][k]
        lower[j][j] = jnp.sqrt(acc)
        for i in range(j + 1, KRY):
            acc = normal[i][j]
            for k in range(j):
                acc = acc - lower[i][k] * lower[j][k]
            lower[i][j] = acc / lower[j][j]
    right_side = [start_norm * hessenberg[0][j] for j in range(KRY)]
    forward = []
    for line in range(KRY):
        accum = right_side[line]
        for other in range(line):
            accum = accum - lower[line][other] * forward[other]
        forward.append(accum / lower[line][line])
    weights = list(forward)
    for line in reversed(range(KRY)):
        accum = forward[line]
        for other in range(line + 1, KRY):
            accum = accum - lower[other][line] * weights[other]
        weights[line] = accum / lower[line][line]
    return weights


def krylov_combination(gram, start_norm):
    size = KRY + 1
    basis = [[-1.0 / start_norm] + [None] * (size - 1)]
    hessenberg = [[None] * KRY for _ in range(KRY + 1)]
    for column in range(KRY):
        image = [None] + basis[column][:-1]
        projections = [quad(image, gram, vector) for vector in basis]
        for line in range(column + 1):
            for a in range(size):
                if basis[line][a] is None:
                    continue
                part = projections[line] * basis[line][a]
                image[a] = -part if image[a] is None else image[a] - part
        remainder = jnp.sqrt(quad(image, gram, image) + EPSILON)
        for line in range(column + 1):
            hessenberg[line][column] = projections[line]
        hessenberg[column + 1][column] = remainder
        if column + 1 < KRY:
            basis.append([None if v is None else v / remainder for v in image])
    weights = cholesky_solve(hessenberg, start_norm)
    total = [None] * size
    for column in range(KRY):
        for a in range(size):
            if basis[column][a] is None:
                continue
            part = weights[column] * basis[column][a]
            total[a] = part if total[a] is None else total[a] + part
    return total


def per_device(start_states, bathymetry, forcing_amp, land_mask):
    seg_local, _, rows, cols = start_states.shape
    segs = seg_local * lax.axis_size("tm")
    count = segs * 3 * rows * lax.axis_size("space") * cols
    wet_cells = (1 - land_mask).astype(jnp.float32)
    order = (lax.axis_index("tm") * seg_local + jnp.arange(seg_local)).astype(jnp.float32)
    cosines = [
        jnp.cos(2.0 * math.pi * (order * STEPS + step) / (segs * STEPS)) for step in range(STEPS)
    ]

    both = jnp.concatenate(
        [jnp.stack([bathymetry, wet_cells, forcing_amp]), start_states.reshape(seg_local * 3, rows, cols)],
        axis=0,
    )
    both = with_halo(both, 1)
    depth_w, wet_w, forcing_w = both[0], both[1], both[2]
    states_w = both[3:].reshape(seg_local, 3, rows + 2 * HALO, cols)

    def interior(wide):
        return wide[:, :, HALO : HALO + rows]

    def run_forward(wide, forcing):
        for step in range(STEPS):
            wide = time_step(wide, cosines[step], depth_w, wet_w, forcing)
        return interior(wide)

    def advance(wide):
        return run_forward(wide, forcing_w)

    following = behind(start_states)
    norms = []
    for newton in range(NEWTON):
        ends, tangent = jax.linearize(advance, states_w)
        krylov = [ahead_wide(ends) - states_w]
        shifted = [ends - following]
        for power in range(KRY):
            image = tangent(krylov[-1])
            shifted.append(image - shifted[-1])
            if power + 1 < KRY:
                krylov.append(ahead_wide(image) - krylov[-1])
        flat = jnp.stack([vector.reshape(-1) for vector in shifted])
        local = jnp.dot(flat, flat.T, precision=lax.Precision.HIGHEST)
        totals = global_sum(jnp.broadcast_to(local[:, :, None], local.shape + (128,)))
        krylov.append(ahead_wide(image) - krylov[-1])
        gram = [[totals[a, b] for b in range(KRY + 1)] for a in range(KRY + 1)]
        squares = gram[0][0]
        norms.append(jnp.sqrt(squares[0] / count))
        start_norm = jnp.sqrt(squares + EPSILON)
        combination = krylov_combination(gram, start_norm)
        for a in range(KRY + 1):
            if combination[a] is not None:
                states_w = states_w + combination[a][0] * krylov[a]
                following = following + combination[a][0] * shifted[a]
    states = interior(states_w)
    ends, back = jax.vjp(run_forward, states_w, forcing_w)
    cotangent = ends - following
    squares = sum_over(jnp.sum(cotangent * cotangent), "space")
    residual = ahead(ends) - states
    cot_states, cot_amp = back(cotangent)
    width = rows + 2 * HALO
    folded = fold_halo(
        jnp.concatenate([cot_states.reshape(seg_local * 3, width, cols), cot_amp[None]], axis=0), 1
    )
    grad_states = folded[: seg_local * 3].reshape(seg_local, 3, rows, cols) - residual
    grad_amp, squares = sum_scatter_tm(folded[seg_local * 3], squares)
    norms.append(jnp.sqrt(squares / count))
    return (states, grad_states, grad_amp, jnp.stack(norms))


def solution(mesh):
    placed = (P("tm", None, "space", None), P("space", None), P("space", None), P("space", None))
    return jax.shard_map(
        per_device,
        mesh=mesh,
        in_specs=placed,
        out_specs=(
            P("tm", None, "space", None),
            P("tm", None, "space", None),
            P("space", "tm"),
            P(),
        ),
        check_vma=False,
    )
```

```python
import math

import jax
import jax.numpy as jnp
from jax import lax
from jax.sharding import PartitionSpec as P

STEPS = 2
KRY = 3
NEWTON = 2


TIME_STEP = 0.4
GRAVITY = 1.0
CORIOLIS = 0.3
FRICTION = 0.05
EPSILON = 1e-06

HALO = 2 * STEPS


def across_cols(field):
    widths = [(0, 0)] * (field.ndim - 1) + [(1, 1)]
    padded = jnp.pad(field, widths)
    return (padded[..., 2:] - padded[..., :-2]) * 0.5


def pad_rows(field):
    widths = [(0, 0)] * (field.ndim - 2) + [(1, 1), (0, 0)]
    return jnp.pad(field, widths)


def momentum(height_rows, height, east_flow, north_flow, wet_cells, push):
    east_slope = (height_rows[..., 2:, :] - height_rows[..., :-2, :]) * 0.5
    north_slope = across_cols(height)
    east_next = wet_cells * (
        east_flow
        + TIME_STEP * (-GRAVITY * east_slope + CORIOLIS * north_flow - FRICTION * east_flow + push)
    )
    north_next = wet_cells * (
        north_flow
        + TIME_STEP * (-GRAVITY * north_slope - CORIOLIS * east_flow - FRICTION * north_flow)
    )
    return (east_next, north_next)


def continuity(height, flux_rows, north_flux, wet_cells):
    divergence = (flux_rows[..., 2:, :] - flux_rows[..., :-2, :]) * 0.5 + across_cols(north_flux)
    return height - TIME_STEP * wet_cells * divergence


def time_step(state, tide_cos, depth, wet, forcing):
    height = state[:, 0]
    east_flow = state[:, 1]
    north_flow = state[:, 2]
    push = forcing * tide_cos[:, None, None]
    east_next, north_next = momentum(pad_rows(height), height, east_flow, north_flow, wet, push)
    total = depth + height
    new_height = continuity(height, pad_rows(total * east_next), total * north_next, wet)
    return jnp.stack([new_height, east_next, north_next], axis=1)


def with_halo(array, dim):
    size, length = lax.axis_size("space"), array.shape[dim]
    down = [(i, i + 1) for i in range(size - 1)]
    up = [(i + 1, i) for i in range(size - 1)]
    last = lax.slice_in_dim(array, length - HALO, length, axis=dim)
    first = lax.slice_in_dim(array, 0, HALO, axis=dim)
    before = lax.ppermute(last, "space", down)
    after = lax.ppermute(first, "space", up)
    return jnp.concatenate([before, array, after], axis=dim)


def fold_halo(array, dim):
    size, length = lax.axis_size("space"), array.shape[dim]
    down = [(i, i + 1) for i in range(size - 1)]
    up = [(i + 1, i) for i in range(size - 1)]
    head = lax.slice_in_dim(array, 0, HALO, axis=dim)
    tail = lax.slice_in_dim(array, length - HALO, length, axis=dim)
    inside = lax.slice_in_dim(array, HALO, length - HALO, axis=dim)
    from_above = lax.ppermute(tail, "space", down)
    from_below = lax.ppermute(head, "space", up)
    rows = inside.shape[dim]
    zeros = jnp.zeros_like(lax.slice_in_dim(inside, 0, rows - 2 * HALO, axis=dim))
    return inside + jnp.concatenate([from_above, zeros, from_below], axis=dim)


def tm_pairs(steps):
    count = lax.axis_size("tm")
    return [(source, (source + steps) % count) for source in range(count)]


def diagonal_pairs(row_step):
    ntm, nsp = lax.axis_size("tm"), lax.axis_size("space")
    pairs = []
    for t in range(ntm):
        for s in range(nsp):
            if 0 <= s + row_step < nsp:
                pairs.append((t * nsp + s, ((t + 1) % ntm) * nsp + s + row_step))
    return pairs


def ahead(segments):
    incoming = lax.ppermute(segments[-1:], "tm", tm_pairs(1))
    return jnp.concatenate([incoming, segments[:-1]], axis=0)


def behind(segments):
    incoming = lax.ppermute(segments[:1], "tm", tm_pairs(-1))
    return jnp.concatenate([segments[1:], incoming], axis=0)


def ahead_wide(segments):
    length = segments.shape[2]
    last = segments[-1:]
    inside = jnp.concatenate([lax.ppermute(last, "tm", tm_pairs(1)), segments[:-1]], axis=0)
    top = lax.ppermute(last[:, :, length - HALO :], ("tm", "space"), diagonal_pairs(1))
    bottom = lax.ppermute(last[:, :, :HALO], ("tm", "space"), diagonal_pairs(-1))
    if segments.shape[0] > 1:
        nsp = lax.axis_size("space")
        rest = segments[:-1]
        top_rest = lax.ppermute(rest[:, :, length - HALO :], "space", [(i, i + 1) for i in range(nsp - 1)])
        bottom_rest = lax.ppermute(rest[:, :, :HALO], "space", [(i + 1, i) for i in range(nsp - 1)])
        top = jnp.concatenate([top, top_rest], axis=0)
        bottom = jnp.concatenate([bottom, bottom_rest], axis=0)
    return jnp.concatenate([top, inside, bottom], axis=2)


def global_sum(value):
    ntm, nsp = lax.axis_size("tm"), lax.axis_size("space")
    for axis, size in (("space", nsp), ("tm", ntm)):
        if size & (size - 1):
            value = lax.psum(value, axis)
            continue
        step = 1
        while step < size:
            value = value + lax.ppermute(value, axis, [(i, i ^ step) for i in range(size)])
            step *= 2
    return value


def sum_over(value, axis):
    size = lax.axis_size(axis)
    if size & (size - 1):
        return lax.psum(value, axis)
    step = 1
    while step < size:
        value = value + lax.ppermute(value, axis, [(i, i ^ step) for i in range(size)])
        step *= 2
    return value


def sum_scatter_tm(value, rider):
    size = lax.axis_size("tm")
    rows, length = value.shape
    lanes = length // size
    if size & (size - 1) or lanes % 128:
        return lax.psum_scatter(value, "tm", scatter_dimension=1, tiled=True), lax.psum(rider, "tm")
    index = lax.axis_index("tm")
    blocks = value.reshape(rows, size, lanes)
    step = 1
    while step < size:
        pairs = blocks.reshape(rows, blocks.shape[1] // 2, 2, lanes)
        upper = (index // step) % 2 == 1
        keep = jnp.where(upper, pairs[:, :, 1], pairs[:, :, 0])
        give = jnp.where(upper, pairs[:, :, 0], pairs[:, :, 1])
        packed = jnp.concatenate([give, jnp.broadcast_to(rider, (rows, 1, lanes))], axis=1)
        got = lax.ppermute(packed, "tm", [(i, i ^ step) for i in range(size)])
        blocks = keep + got[:, :-1]
        rider = rider + got[0, -1, 0]
        step *= 2
    return blocks.reshape(rows, lanes), rider


def quad(left, gram, right):
    total = None
    for a, lv in enumerate(left):
        if lv is None:
            continue
        for b, rv in enumerate(right):
            if rv is None:
                continue
            term = lv * gram[a][b] * rv
            total = term if total is None else total + term
    return total


def cholesky_solve(hessenberg, start_norm):
    normal = [[None] * KRY for _ in range(KRY)]
    for i in range(KRY):
        for j in range(i + 1):
            acc = None
            for k in range(KRY + 1):
                if hessenberg[k][i] is None or hessenberg[k][j] is None:
                    continue
                term = hessenberg[k][i] * hessenberg[k][j]
                acc = term if acc is None else acc + term
            normal[i][j] = acc
    lower = [[None] * KRY for _ in range(KRY)]
    for j in range(KRY):
        acc = normal[j][j]
        for k in range(j):
            acc = acc - lower[j][k] * lower[j][k]
        lower[j][j] = jnp.sqrt(acc)
        for i in range(j + 1, KRY):
            acc = normal[i][j]
            for k in range(j):
                acc = acc - lower[i][k] * lower[j][k]
            lower[i][j] = acc / lower[j][j]
    right_side = [start_norm * hessenberg[0][j] for j in range(KRY)]
    forward = []
    for line in range(KRY):
        accum = right_side[line]
        for other in range(line):
            accum = accum - lower[line][other] * forward[other]
        forward.append(accum / lower[line][line])
    weights = list(forward)
    for line in reversed(range(KRY)):
        accum = forward[line]
        for other in range(line + 1, KRY):
            accum = accum - lower[other][line] * weights[other]
        weights[line] = accum / lower[line][line]
    return weights


def krylov_combination(gram, start_norm):
    size = KRY + 1
    basis = [[-1.0 / start_norm] + [None] * (size - 1)]
    hessenberg = [[None] * KRY for _ in range(KRY + 1)]
    for column in range(KRY):
        image = [None] + basis[column][:-1]
        projections = [quad(image, gram, vector) for vector in basis]
        for line in range(column + 1):
            for a in range(size):
                if basis[line][a] is None:
                    continue
                part = projections[line] * basis[line][a]
                image[a] = -part if image[a] is None else image[a] - part
        remainder = jnp.sqrt(quad(image, gram, image) + EPSILON)
        for line in range(column + 1):
            hessenberg[line][column] = projections[line]
        hessenberg[column + 1][column] = remainder
        if column + 1 < KRY:
            basis.append([None if v is None else v / remainder for v in image])
    weights = cholesky_solve(hessenberg, start_norm)
    total = [None] * size
    for column in range(KRY):
        for a in range(size):
            if basis[column][a] is None:
                continue
            part = weights[column] * basis[column][a]
            total[a] = part if total[a] is None else total[a] + part
    return total


def per_device(start_states, bathymetry, forcing_amp, land_mask):
    seg_local, _, rows, cols = start_states.shape
    segs = seg_local * lax.axis_size("tm")
    count = segs * 3 * rows * lax.axis_size("space") * cols
    wet_cells = (1 - land_mask).astype(jnp.float32)
    order = (lax.axis_index("tm") * seg_local + jnp.arange(seg_local)).astype(jnp.float32)
    cosines = [
        jnp.cos(2.0 * math.pi * (order * STEPS + step) / (segs * STEPS)) for step in range(STEPS)
    ]

    both = jnp.concatenate(
        [jnp.stack([bathymetry, wet_cells, forcing_amp]), start_states.reshape(seg_local * 3, rows, cols)],
        axis=0,
    )
    both = with_halo(both, 1)
    depth_w, wet_w, forcing_w = both[0], both[1], both[2]
    states_w = both[3:].reshape(seg_local, 3, rows + 2 * HALO, cols)

    def interior(wide):
        return wide[:, :, HALO : HALO + rows]

    def run_forward(wide, forcing):
        for step in range(STEPS):
            wide = time_step(wide, cosines[step], depth_w, wet_w, forcing)
        return interior(wide)

    def advance(wide):
        return run_forward(wide, forcing_w)

    following = behind(start_states)
    def newton_step(carry, unused):
        states_w, following = carry
        ends, tangent = jax.linearize(advance, states_w)
        krylov = [ahead_wide(ends) - states_w]
        shifted = [ends - following]
        for power in range(KRY):
            image = tangent(krylov[-1])
            shifted.append(image - shifted[-1])
            if power + 1 < KRY:
                krylov.append(ahead_wide(image) - krylov[-1])
        flat = jnp.stack([vector.reshape(-1) for vector in shifted])
        local = jnp.dot(flat, flat.T, precision=lax.Precision.HIGHEST)
        totals = global_sum(jnp.broadcast_to(local[:, :, None], local.shape + (128,)))
        krylov.append(ahead_wide(image) - krylov[-1])
        gram = [[totals[a, b] for b in range(KRY + 1)] for a in range(KRY + 1)]
        squares = gram[0][0]
        start_norm = jnp.sqrt(squares + EPSILON)
        combination = krylov_combination(gram, start_norm)
        for a in range(KRY + 1):
            if combination[a] is not None:
                states_w = states_w + combination[a][0] * krylov[a]
                following = following + combination[a][0] * shifted[a]
        return (states_w, following), jnp.sqrt(squares[0] / count)

    (states_w, following), newton_norms = lax.scan(newton_step, (states_w, following), None, length=NEWTON)
    norms = [newton_norms[n] for n in range(NEWTON)]
    states = interior(states_w)
    ends, back = jax.vjp(run_forward, states_w, forcing_w)
    cotangent = ends - following
    squares = sum_over(jnp.sum(cotangent * cotangent), "space")
    residual = ahead(ends) - states
    cot_states, cot_amp = back(cotangent)
    width = rows + 2 * HALO
    folded = fold_halo(
        jnp.concatenate([cot_states.reshape(seg_local * 3, width, cols), cot_amp[None]], axis=0), 1
    )
    grad_states = folded[: seg_local * 3].reshape(seg_local, 3, rows, cols) - residual
    grad_amp, squares = sum_scatter_tm(folded[seg_local * 3], squares)
    norms.append(jnp.sqrt(squares / count))
    return (states, grad_states, grad_amp, jnp.stack(norms))


def solution(mesh):
    placed = (P("tm", None, "space", None), P("space", None), P("space", None), P("space", None))
    return jax.shard_map(
        per_device,
        mesh=mesh,
        in_specs=placed,
        out_specs=(
            P("tm", None, "space", None),
            P("tm", None, "space", None),
            P("space", "tm"),
            P(),
        ),
        check_vma=False,
    )
```

```python
import math

import jax
import jax.numpy as jnp
from jax import lax
from jax.sharding import PartitionSpec as P

STEPS = 2
KRY = 3
NEWTON = 2


TIME_STEP = 0.4
GRAVITY = 1.0
CORIOLIS = 0.3
FRICTION = 0.05
EPSILON = 1e-06

HALO = 2 * STEPS


def across_cols(field):
    widths = [(0, 0)] * (field.ndim - 1) + [(1, 1)]
    padded = jnp.pad(field, widths)
    return (padded[..., 2:] - padded[..., :-2]) * 0.5


def pad_rows(field):
    widths = [(0, 0)] * (field.ndim - 2) + [(1, 1), (0, 0)]
    return jnp.pad(field, widths)


def momentum(height_rows, height, east_flow, north_flow, wet_cells, push):
    east_slope = (height_rows[..., 2:, :] - height_rows[..., :-2, :]) * 0.5
    north_slope = across_cols(height)
    east_next = wet_cells * (
        east_flow
        + TIME_STEP * (-GRAVITY * east_slope + CORIOLIS * north_flow - FRICTION * east_flow + push)
    )
    north_next = wet_cells * (
        north_flow
        + TIME_STEP * (-GRAVITY * north_slope - CORIOLIS * east_flow - FRICTION * north_flow)
    )
    return (east_next, north_next)


def continuity(height, flux_rows, north_flux, wet_cells):
    divergence = (flux_rows[..., 2:, :] - flux_rows[..., :-2, :]) * 0.5 + across_cols(north_flux)
    return height - TIME_STEP * wet_cells * divergence


def time_step(state, tide_cos, depth, wet, forcing):
    height = state[:, 0]
    east_flow = state[:, 1]
    north_flow = state[:, 2]
    push = forcing * tide_cos[:, None, None]
    east_next, north_next = momentum(pad_rows(height), height, east_flow, north_flow, wet, push)
    total = depth + height
    new_height = continuity(height, pad_rows(total * east_next), total * north_next, wet)
    return jnp.stack([new_height, east_next, north_next], axis=1)


def with_halo(array, dim):
    size, length = lax.axis_size("space"), array.shape[dim]
    down = [(i, i + 1) for i in range(size - 1)]
    up = [(i + 1, i) for i in range(size - 1)]
    last = lax.slice_in_dim(array, length - HALO, length, axis=dim)
    first = lax.slice_in_dim(array, 0, HALO, axis=dim)
    before = lax.ppermute(last, "space", down)
    after = lax.ppermute(first, "space", up)
    return jnp.concatenate([before, array, after], axis=dim)


def fold_halo(array, dim):
    size, length = lax.axis_size("space"), array.shape[dim]
    down = [(i, i + 1) for i in range(size - 1)]
    up = [(i + 1, i) for i in range(size - 1)]
    head = lax.slice_in_dim(array, 0, HALO, axis=dim)
    tail = lax.slice_in_dim(array, length - HALO, length, axis=dim)
    inside = lax.slice_in_dim(array, HALO, length - HALO, axis=dim)
    from_above = lax.ppermute(tail, "space", down)
    from_below = lax.ppermute(head, "space", up)
    rows = inside.shape[dim]
    zeros = jnp.zeros_like(lax.slice_in_dim(inside, 0, rows - 2 * HALO, axis=dim))
    return inside + jnp.concatenate([from_above, zeros, from_below], axis=dim)


def tm_pairs(steps):
    count = lax.axis_size("tm")
    return [(source, (source + steps) % count) for source in range(count)]


def diagonal_pairs(row_step):
    ntm, nsp = lax.axis_size("tm"), lax.axis_size("space")
    pairs = []
    for t in range(ntm):
        for s in range(nsp):
            if 0 <= s + row_step < nsp:
                pairs.append((t * nsp + s, ((t + 1) % ntm) * nsp + s + row_step))
    return pairs


def ahead(segments):
    incoming = lax.ppermute(segments[-1:], "tm", tm_pairs(1))
    return jnp.concatenate([incoming, segments[:-1]], axis=0)


def behind(segments):
    incoming = lax.ppermute(segments[:1], "tm", tm_pairs(-1))
    return jnp.concatenate([segments[1:], incoming], axis=0)


def ahead_wide(segments):
    length = segments.shape[2]
    last = segments[-1:]
    inside = jnp.concatenate([lax.ppermute(last, "tm", tm_pairs(1)), segments[:-1]], axis=0)
    top = lax.ppermute(last[:, :, length - HALO :], ("tm", "space"), diagonal_pairs(1))
    bottom = lax.ppermute(last[:, :, :HALO], ("tm", "space"), diagonal_pairs(-1))
    if segments.shape[0] > 1:
        nsp = lax.axis_size("space")
        rest = segments[:-1]
        top_rest = lax.ppermute(rest[:, :, length - HALO :], "space", [(i, i + 1) for i in range(nsp - 1)])
        bottom_rest = lax.ppermute(rest[:, :, :HALO], "space", [(i + 1, i) for i in range(nsp - 1)])
        top = jnp.concatenate([top, top_rest], axis=0)
        bottom = jnp.concatenate([bottom, bottom_rest], axis=0)
    return jnp.concatenate([top, inside, bottom], axis=2)


def global_sum(value):
    ntm, nsp = lax.axis_size("tm"), lax.axis_size("space")
    for axis, size in (("space", nsp), ("tm", ntm)):
        if size & (size - 1):
            value = lax.psum(value, axis)
            continue
        step = 1
        while step < size:
            value = value + lax.ppermute(value, axis, [(i, i ^ step) for i in range(size)])
            step *= 2
    return value


def global_sum_lanes(value, lanes=128):
    rounds = []
    for axis in ("space", "tm"):
        size = lax.axis_size(axis)
        if size & (size - 1):
            return jnp.broadcast_to(global_sum(value)[..., None], value.shape + (lanes,))
        step = 1
        while step < size:
            rounds.append((axis, [(i, i ^ step) for i in range(size)]))
            step *= 2
    for axis, pairs in rounds[:-1]:
        value = value + lax.ppermute(value, axis, pairs)
    wide = jnp.broadcast_to(value[..., None], value.shape + (lanes,))
    axis, pairs = rounds[-1]
    return wide + lax.ppermute(wide, axis, pairs)


def sum_over(value, axis):
    size = lax.axis_size(axis)
    if size & (size - 1):
        return lax.psum(value, axis)
    step = 1
    while step < size:
        value = value + lax.ppermute(value, axis, [(i, i ^ step) for i in range(size)])
        step *= 2
    return value


def sum_scatter_tm(value, rider):
    size = lax.axis_size("tm")
    rows, length = value.shape
    lanes = length // size
    if size & (size - 1) or lanes % 128:
        return lax.psum_scatter(value, "tm", scatter_dimension=1, tiled=True), lax.psum(rider, "tm")
    index = lax.axis_index("tm")
    blocks = value.reshape(rows, size, lanes)
    step = 1
    while step < size:
        pairs = blocks.reshape(rows, blocks.shape[1] // 2, 2, lanes)
        upper = (index // step) % 2 == 1
        keep = jnp.where(upper, pairs[:, :, 1], pairs[:, :, 0])
        give = jnp.where(upper, pairs[:, :, 0], pairs[:, :, 1])
        packed = jnp.concatenate([give, jnp.broadcast_to(rider, (rows, 1, lanes))], axis=1)
        got = lax.ppermute(packed, "tm", [(i, i ^ step) for i in range(size)])
        blocks = keep + got[:, :-1]
        rider = rider + got[0, -1, 0]
        step *= 2
    return blocks.reshape(rows, lanes), rider


def quad(left, gram, right):
    total = None
    for a, lv in enumerate(left):
        if lv is None:
            continue
        for b, rv in enumerate(right):
            if rv is None:
                continue
            term = lv * gram[a][b] * rv
            total = term if total is None else total + term
    return total


def cholesky_solve(hessenberg, start_norm):
    normal = [[None] * KRY for _ in range(KRY)]
    for i in range(KRY):
        for j in range(i + 1):
            acc = None
            for k in range(KRY + 1):
                if hessenberg[k][i] is None or hessenberg[k][j] is None:
                    continue
                term = hessenberg[k][i] * hessenberg[k][j]
                acc = term if acc is None else acc + term
            normal[i][j] = acc
    lower = [[None] * KRY for _ in range(KRY)]
    for j in range(KRY):
        acc = normal[j][j]
        for k in range(j):
            acc = acc - lower[j][k] * lower[j][k]
        lower[j][j] = jnp.sqrt(acc)
        for i in range(j + 1, KRY):
            acc = normal[i][j]
            for k in range(j):
                acc = acc - lower[i][k] * lower[j][k]
            lower[i][j] = acc / lower[j][j]
    right_side = [start_norm * hessenberg[0][j] for j in range(KRY)]
    forward = []
    for line in range(KRY):
        accum = right_side[line]
        for other in range(line):
            accum = accum - lower[line][other] * forward[other]
        forward.append(accum / lower[line][line])
    weights = list(forward)
    for line in reversed(range(KRY)):
        accum = forward[line]
        for other in range(line + 1, KRY):
            accum = accum - lower[other][line] * weights[other]
        weights[line] = accum / lower[line][line]
    return weights


def krylov_combination(gram, start_norm):
    size = KRY + 1
    basis = [[-1.0 / start_norm] + [None] * (size - 1)]
    hessenberg = [[None] * KRY for _ in range(KRY + 1)]
    for column in range(KRY):
        image = [None] + basis[column][:-1]
        projections = [quad(image, gram, vector) for vector in basis]
        for line in range(column + 1):
            for a in range(size):
                if basis[line][a] is None:
                    continue
                part = projections[line] * basis[line][a]
                image[a] = -part if image[a] is None else image[a] - part
        remainder = jnp.sqrt(quad(image, gram, image) + EPSILON)
        for line in range(column + 1):
            hessenberg[line][column] = projections[line]
        hessenberg[column + 1][column] = remainder
        if column + 1 < KRY:
            basis.append([None if v is None else v / remainder for v in image])
    weights = cholesky_solve(hessenberg, start_norm)
    total = [None] * size
    for column in range(KRY):
        for a in range(size):
            if basis[column][a] is None:
                continue
            part = weights[column] * basis[column][a]
            total[a] = part if total[a] is None else total[a] + part
    return total


def per_device(start_states, bathymetry, forcing_amp, land_mask):
    seg_local, _, rows, cols = start_states.shape
    segs = seg_local * lax.axis_size("tm")
    count = segs * 3 * rows * lax.axis_size("space") * cols
    wet_cells = (1 - land_mask).astype(jnp.float32)
    order = (lax.axis_index("tm") * seg_local + jnp.arange(seg_local)).astype(jnp.float32)
    cosines = [
        jnp.cos(2.0 * math.pi * (order * STEPS + step) / (segs * STEPS)) for step in range(STEPS)
    ]

    both = jnp.concatenate(
        [jnp.stack([bathymetry, wet_cells, forcing_amp]), start_states.reshape(seg_local * 3, rows, cols)],
        axis=0,
    )
    both = with_halo(both, 1)
    depth_w, wet_w, forcing_w = both[0], both[1], both[2]
    states_w = both[3:].reshape(seg_local, 3, rows + 2 * HALO, cols)

    def interior(wide):
        return wide[:, :, HALO : HALO + rows]

    def run_forward(wide, forcing):
        for step in range(STEPS):
            wide = time_step(wide, cosines[step], depth_w, wet_w, forcing)
        return interior(wide)

    def advance(wide):
        return run_forward(wide, forcing_w)

    following = behind(start_states)
    def newton_step(carry, unused):
        states_w, following = carry
        ends, tangent = jax.linearize(advance, states_w)
        krylov = [ahead_wide(ends) - states_w]
        shifted = [ends - following]
        for power in range(KRY):
            image = tangent(krylov[-1])
            shifted.append(image - shifted[-1])
            if power + 1 < KRY:
                krylov.append(ahead_wide(image) - krylov[-1])
        flat = jnp.stack([vector.reshape(-1) for vector in shifted])
        local = jnp.dot(flat, flat.T, precision=lax.Precision.HIGHEST)
        totals = global_sum_lanes(local)
        krylov.append(ahead_wide(image) - krylov[-1])
        gram = [[totals[a, b] for b in range(KRY + 1)] for a in range(KRY + 1)]
        squares = gram[0][0]
        start_norm = jnp.sqrt(squares + EPSILON)
        combination = krylov_combination(gram, start_norm)
        for a in range(KRY + 1):
            if combination[a] is not None:
                states_w = states_w + combination[a][0] * krylov[a]
                following = following + combination[a][0] * shifted[a]
        return (states_w, following), jnp.sqrt(squares[0] / count)

    (states_w, following), newton_norms = lax.scan(newton_step, (states_w, following), None, length=NEWTON)
    norms = [newton_norms[n] for n in range(NEWTON)]
    states = interior(states_w)
    ends, back = jax.vjp(run_forward, states_w, forcing_w)
    cotangent = ends - following
    squares = sum_over(jnp.sum(cotangent * cotangent), "space")
    residual = ahead(ends) - states
    cot_states, cot_amp = back(cotangent)
    width = rows + 2 * HALO
    folded = fold_halo(
        jnp.concatenate([cot_states.reshape(seg_local * 3, width, cols), cot_amp[None]], axis=0), 1
    )
    grad_states = folded[: seg_local * 3].reshape(seg_local, 3, rows, cols) - residual
    grad_amp, squares = sum_scatter_tm(folded[seg_local * 3], squares)
    norms.append(jnp.sqrt(squares / count))
    return (states, grad_states, grad_amp, jnp.stack(norms))


def solution(mesh):
    placed = (P("tm", None, "space", None), P("space", None), P("space", None), P("space", None))
    return jax.shard_map(
        per_device,
        mesh=mesh,
        in_specs=placed,
        out_specs=(
            P("tm", None, "space", None),
            P("tm", None, "space", None),
            P("space", "tm"),
            P(),
        ),
        check_vma=False,
    )
```
